512 devices in a mesh: dp: 32 (over x, y, core), expert: 16 (over z).
Axes of the slice: x: 4, y: 4, z: 16, core: 2. Of those that a mesh axis runs over, the one named last changes fastest.
Arguments:
- tokens: bfloat16 [4096, 2048], P('dp', 'expert'), may hold values from -6 to 6
- route_weight: bfloat16 [4096, 8], P('dp'), may hold values from 0.049804688 to 0.44921875
- expert_ids: int32 [4096, 8], P('dp'), may hold values from 0 to 127, all different within a row; in each aligned block of 128 rows (0 to 127, 128 to 255, ...) at most 16 rows name the same one
- gate_weight: bfloat16 [16, 6144, 2048], P('expert', 'dp'), may hold values from -0.125 to 0.125
- up_weight: bfloat16 [16, 6144, 2048], P('expert', 'dp'), may hold values from -0.125 to 0.125
- down_weight: bfloat16 [16, 6144, 2048], P('expert', 'dp'), may hold values from -0.21875 to 0.21875
- grad_output: bfloat16 [4096, 2048], P('dp', 'expert'), may hold values from -1.75 to 1.75
Outputs:
- mixed: bfloat16 [4096, 2048], P('dp', 'expert')
- grad_tokens: bfloat16 [4096, 2048], P('dp', 'expert')
- grad_route: float32 [4096, 8], P(('dp', 'expert'))
- grad_gate: bfloat16 [16, 6144, 2048], P('expert', 'dp')
- grad_up: bfloat16 [16, 6144, 2048], P('expert', 'dp')
- grad_down: bfloat16 [16, 6144, 2048], P('expert', 'dp')
The draws below stay inside these ranges and needn't reach their ends.
Inputs may be any that keep to these rules, and one draw needn't show every extreme that they name: `expert_ids`: each token names 8 different experts; among the 128 tokens of one device's aligned block no expert is named more than 16 times, a bound that some block reaches.
All inputs are finite; a program needn't handle non-finite values.
Results may differ from the reference program's by a relative error of at most 0.015.
Values may be sent and summed in bfloat16 or wider, within the bound.
No kernel may reach another device: no remote copies, remote signals or barrier semaphores. Data moves between devices by JAX's collectives and lax.ppermute only.
A program may use at most 64 MiB of HBM per device.

```python
import math
import jax
import jax.numpy as jnp
import numpy as np
from jax import lax

D = 2048
FF = 768
TOPK = 8
PIECES = 4
TOK_DEV = 128
FFD = 192
EXP_DEV = 8
EXPERTS = 128
CAP = 16
TOKENS = 4096
N_DP = 32
N_EXPERT = 16


def block_levels(rng, shape, split, smallest, top_value):
    factor_of = 1.0
    for dim, shards_of in split:
        steps = jax.random.uniform(jax.random.fold_in(jax.random.fold_in(rng, 6), dim), (shards_of,), jnp.float32, smallest / len(split), top_value / len(split))
        factor_of = factor_of * jnp.repeat(jnp.exp(steps), shape[dim] // shards_of).reshape((-1,) + (1,) * (len(shape) - 1 - dim))
    return factor_of


def assign_block(key, own, number, rows, count, top, reach, skew):
    order = jax.random.permutation(key, count)
    crowded, usual = load_shares(count, rows * top, reach, skew, True), load_shares(count, rows * top, reach, skew, False)
    places = jnp.arange(count)

    def named(lengths, offset_by):
        used = int((lengths > 0).sum())
        fixed = max(1, used // 4)
        passed = fixed + (places - fixed + offset_by * (used - fixed)) % max(1, count - fixed)
        return jnp.zeros((count,), jnp.int32).at[order[jnp.where(places < fixed, places, passed)]].set(jnp.asarray(lengths, jnp.int32))

    lengths = jnp.where(number % 4 == 0, named(crowded, number // 4), named(usual, number - number // 4 - 1))
    mixed = jax.random.permutation(jax.random.fold_in(own, 3), count)
    giver, receiver = mixed[0:count // 2 * 2:2], mixed[1:count // 2 * 2:2]
    margin = jnp.minimum(lengths[giver] - 1, reach - lengths[receiver]) // 2
    margin = jnp.where((giver == order[0]) | (receiver == order[0]) | (lengths[receiver] == 0), 0, jnp.maximum(margin, 0))
    passed = jax.random.randint(jax.random.fold_in(own, 4), (count // 2,), 0, 1 << 20) % (margin + 1)
    lengths = lengths.at[giver].add(-passed).at[receiver].add(passed)
    items = jnp.searchsorted(jnp.cumsum(lengths), jnp.arange(rows * top), side="right").astype(jnp.int32)
    table = items.reshape(top, rows).T
    table = table[jax.random.permutation(jax.random.fold_in(own, 1), rows)]
    offset_by = jax.random.randint(jax.random.fold_in(own, 2), (rows, 1), 0, top)
    return jnp.take_along_axis(table, (jnp.arange(top)[None, :] + offset_by) % top, axis=1)


def load_shares(number_of, total, most, lean, full):
    weights = [(1 << 20) // math.isqrt(rank ** lean) + 1 for rank in range(1, number_of + 1)]
    largest = most if full else min(most, max(-(-total // number_of), total * weights[0] // sum(weights)))
    least = 1 if total - largest >= number_of - 1 else 0
    holding, rest = [largest] + [least] * (number_of - 1), total - largest - least * (number_of - 1)
    while rest > 0:
        free = [i for i in range(1, number_of) if holding[i] < largest] or [i for i in range(1, number_of) if holding[i] < most]
        pool, left = sum([weights[i] for i in free]), rest
        for i in free:
            extra = min(most - holding[i], max(1, left * weights[i] // pool), rest)
            holding[i] = holding[i] + extra
            rest = rest - extra
    return np.array(holding)


def noise(rng, shape, spread, limit, pieces=(), kind=jnp.bfloat16):
    entries = spread * jax.random.normal(rng, shape, jnp.float32)
    if pieces:
        entries = entries * block_levels(rng, shape, pieces, -0.22, 0.18)
    return jnp.clip(entries, -limit, limit).astype(kind)


def setup_inputs(seed: int = 0) -> dict:
    splits = jax.random.split(jax.random.key(seed), 8)
    tokens = noise(splits[0], (TOKENS, D), 1.0, 6.0, ((0, 32), (1, 16)))
    route_weight = jnp.clip(0.049804688 + 0.39941406 * jax.random.uniform(splits[1], (TOKENS, TOPK), jnp.float32) ** block_levels(splits[1], (TOKENS, TOPK), ((0, 32),), -0.2, 0.2), 0.049804688, 0.44921875).astype(jnp.bfloat16)
    expert_ids_keys = jax.random.split(jax.random.fold_in(splits[2], 1), TOKENS // TOK_DEV)
    expert_ids_turns = jax.random.permutation(jax.random.fold_in(splits[2], 3), TOKENS // TOK_DEV)
    expert_ids = jax.vmap(lambda own, number: assign_block(jax.random.fold_in(splits[2], 2), own, number, TOK_DEV, EXPERTS, TOPK, CAP, 2))(expert_ids_keys, expert_ids_turns).reshape((TOKENS, TOPK))
    gate_weight = noise(splits[3], (N_EXPERT, EXP_DEV * FF, D), D ** -0.5, 0.125, ((0, 16), (1, 32)))
    up_weight = noise(splits[4], (N_EXPERT, EXP_DEV * FF, D), D ** -0.5, 0.125, ((0, 16), (1, 32)))
    down_weight = noise(splits[5], (N_EXPERT, EXP_DEV * FF, D), FF ** -0.5, 0.21875, ((0, 16), (1, 32)))
    grad_output = noise(splits[6], (TOKENS, D), 0.3, 1.75, ((0, 32), (1, 16)))
    return dict(tokens=tokens, route_weight=route_weight, expert_ids=expert_ids, gate_weight=gate_weight, up_weight=up_weight, down_weight=down_weight, grad_output=grad_output)


def contract_last(left_side, right_side):
    return lax.dot_general(left_side, right_side, (((1,), (1,)), ((), ())), preferred_element_type=jnp.float32)


def contract_first(left_side, right_side):
    return lax.dot_general(left_side, right_side, (((0,), (0,)), ((), ())), preferred_element_type=jnp.float32)


def silu_parts(gate_act):
    sigmoid_val = jax.nn.sigmoid(gate_act)
    return gate_act * sigmoid_val, sigmoid_val * (1.0 + gate_act * (1.0 - sigmoid_val))


def slot_tables(expert_ids):
    block_rows = TOK_DEV * TOPK
    blocked = expert_ids.reshape(N_DP, block_rows)
    chosen = (blocked[:, :, None] == jnp.arange(EXPERTS, dtype=jnp.int32)[None, None, :]).astype(jnp.int32)
    slot_ranks = jnp.sum(chosen * (jnp.cumsum(chosen, axis=1) - 1), axis=2)
    starts = jnp.arange(N_DP, dtype=jnp.int32)[:, None] * CAP
    position = (starts + slot_ranks).reshape(-1).astype(jnp.int32)
    flat_ids = expert_ids.reshape(-1).astype(jnp.int32)
    row_index = jnp.arange(TOKENS * TOPK, dtype=jnp.int32)
    row_of = jnp.zeros((EXPERTS, N_DP * CAP), jnp.int32).at[flat_ids, position].set(row_index)
    slot_live = jnp.zeros((EXPERTS, N_DP * CAP), jnp.int32).at[flat_ids, position].set(jnp.ones_like(row_index))
    return row_of, slot_live


def reference(tokens, route_weight, expert_ids, gate_weight, up_weight, down_weight, grad_output):
    row_of, slot_live = slot_tables(expert_ids)
    flat_weight = route_weight.reshape(-1)
    gate_all = gate_weight.reshape(EXPERTS, PIECES, FFD, D)
    up_all = up_weight.reshape(EXPERTS, PIECES, FFD, D)
    down_all = down_weight.reshape(EXPERTS, PIECES, FFD, D)

    def per_expert(carry, item):
        mixed_sum, token_sum, route_sum = carry
        slot_row, live_row, gate_block, up_block, down_block = item
        slot_token = slot_row // TOPK
        keep_mask = live_row.astype(tokens.dtype)[:, None]
        slot_rows = tokens[slot_token] * keep_mask
        slot_grads = grad_output[slot_token] * keep_mask
        slot_scale = flat_weight[slot_row] * live_row.astype(route_weight.dtype)
        weight_wide = slot_scale.astype(jnp.float32)[:, None]
        scaled_grad = (weight_wide * slot_grads.astype(jnp.float32)).astype(jnp.bfloat16)
        out_total = jnp.zeros((N_DP * CAP, D), jnp.float32)
        grad_total = jnp.zeros((N_DP * CAP, D), jnp.float32)
        term_total = jnp.zeros((N_DP * CAP,), jnp.float32)
        gate_list = []
        up_list = []
        down_list = []
        for section in range(PIECES):
            gate_act = contract_last(slot_rows, gate_block[section])
            up_act = contract_last(slot_rows, up_block[section])
            active, silu_slope = silu_parts(gate_act)
            hidden = (active * up_act).astype(jnp.bfloat16)
            partial_out = jnp.dot(hidden, down_block[section], preferred_element_type=jnp.float32)
            piece_out = lax.optimization_barrier((weight_wide * partial_out).astype(jnp.bfloat16))
            out_total = out_total + piece_out.astype(jnp.float32)
            into_hidden = contract_last(slot_grads, down_block[section])
            route_term = jnp.sum(into_hidden * hidden.astype(jnp.float32), axis=1)
            route_term = lax.optimization_barrier(route_term.astype(jnp.bfloat16))
            term_total = term_total + route_term.astype(jnp.float32)
            hidden_grad = weight_wide * into_hidden
            gate_grad = (hidden_grad * up_act * silu_slope).astype(jnp.bfloat16)
            up_grad = (hidden_grad * active).astype(jnp.bfloat16)
            row_grad = jnp.dot(gate_grad, gate_block[section], preferred_element_type=jnp.float32) + jnp.dot(up_grad, up_block[section], preferred_element_type=jnp.float32)
            row_grad = lax.optimization_barrier(row_grad.astype(jnp.bfloat16))
            grad_total = grad_total + row_grad.astype(jnp.float32)
            gate_list.append(contract_first(gate_grad, slot_rows).astype(jnp.bfloat16))
            up_list.append(contract_first(up_grad, slot_rows).astype(jnp.bfloat16))
            down_list.append(contract_first(hidden, scaled_grad).astype(jnp.bfloat16))
        mixed_sum = mixed_sum.at[slot_token].add(out_total)
        token_sum = token_sum.at[slot_token].add(grad_total)
        route_sum = route_sum.at[slot_row].add(term_total)
        return (mixed_sum, token_sum, route_sum), (jnp.stack(gate_list), jnp.stack(up_list), jnp.stack(down_list))

    initial = (jnp.zeros((TOKENS, D), jnp.float32), jnp.zeros((TOKENS, D), jnp.float32), jnp.zeros((TOKENS * TOPK,), jnp.float32))
    totals, grads = lax.scan(per_expert, initial, (row_of, slot_live, gate_all, up_all, down_all))
    mixed_sum, token_sum, route_sum = totals
    gate_grads, up_grads, down_grads = grads
    grad_shape = (N_EXPERT, EXP_DEV * FF, D)
    return (mixed_sum.astype(jnp.bfloat16), token_sum.astype(jnp.bfloat16), route_sum.reshape(TOKENS, TOPK), gate_grads.reshape(grad_shape), up_grads.reshape(grad_shape), down_grads.reshape(grad_shape))
```

```python
import jax
import jax.numpy as jnp
from jax import lax
from jax.sharding import PartitionSpec as P

PIECES = 4
PAD = 128


def contract_last(left_side, right_side):
    return lax.dot_general(
        left_side, right_side, (((1,), (1,)), ((), ())), preferred_element_type=jnp.float32
    )


def contract_first(left_side, right_side):
    return lax.dot_general(
        left_side, right_side, (((0,), (0,)), ((), ())), preferred_element_type=jnp.float32
    )


def silu_parts(gate_act):
    sigmoid_val = jax.nn.sigmoid(gate_act)
    return (gate_act * sigmoid_val, sigmoid_val * (1.0 + gate_act * (1.0 - sigmoid_val)))


def column_block(values, dtype):
    lane = jnp.arange(PAD, dtype=jnp.int32)[None, :] == 0
    return jnp.where(lane, values.astype(dtype)[:, None], jnp.zeros((), dtype))


def on_device(tokens, route_weight, expert_ids, gate_weight, up_weight, down_weight, grad_output):
    groups = lax.axis_size("expert")
    group_index = lax.axis_index("expert")
    data_size = lax.axis_size("dp")
    exp_local = data_size // PIECES
    tok_local, topk_count = expert_ids.shape
    capacity = min(tok_local, 2 * tok_local * topk_count // (exp_local * groups))
    part_width = tokens.shape[1]
    both = jnp.concatenate([tokens, grad_output], axis=1)
    gathered = lax.all_gather(both, "expert", axis=0, tiled=False)
    gathered = gathered.reshape(groups, tok_local, 2, part_width)
    full_both = jnp.transpose(gathered, (1, 2, 0, 3)).reshape(tok_local, 2 * groups * part_width)
    feature_width = groups * part_width
    gate_piece = gate_weight[0]
    up_piece = up_weight[0]
    down_piece = down_weight[0]
    flat_ids = expert_ids.reshape(-1)
    row_count = flat_ids.shape[0]
    owned_rows = flat_ids // exp_local == group_index
    local_ids = flat_ids % exp_local
    chosen = (
        (local_ids[:, None] == jnp.arange(exp_local, dtype=jnp.int32)[None, :])
        & owned_rows[:, None]
    ).astype(jnp.int32)
    slot_ranks = jnp.sum(chosen * (jnp.cumsum(chosen, axis=0) - 1), axis=1)
    slot_count = exp_local * capacity
    slot_pos = jnp.where(owned_rows, local_ids * capacity + slot_ranks, slot_count)
    row_index = jnp.arange(row_count, dtype=jnp.int32)
    row_of = jnp.zeros((slot_count,), jnp.int32).at[slot_pos].set(row_index, mode="drop")
    slot_live = (
        jnp.zeros((slot_count,), jnp.int32).at[slot_pos].set(jnp.ones_like(row_index), mode="drop")
    )
    token_of = row_of // topk_count
    keep_mask = slot_live.astype(tokens.dtype)[:, None]
    slot_weight = route_weight.reshape(-1)[row_of] * slot_live.astype(route_weight.dtype)

    def spread(values):
        trailing = values.shape[1:]
        grouped = values.reshape((exp_local, 1, capacity) + trailing)
        return jnp.broadcast_to(grouped, (exp_local, PIECES, capacity) + trailing).reshape(
            (data_size, capacity) + trailing
        )

    send_buf = jnp.concatenate(
        [full_both[token_of] * keep_mask, column_block(slot_weight, tokens.dtype)], axis=1
    )
    recv_buf = lax.all_to_all(spread(send_buf), "dp", split_axis=0, concat_axis=0, tiled=True)
    recv_buf = recv_buf.reshape(-1, 2 * feature_width + PAD)
    slot_rows = recv_buf[:, :feature_width]
    slot_grads = recv_buf[:, feature_width : 2 * feature_width]
    slot_scale = recv_buf[:, 2 * feature_width]
    weight_wide = slot_scale.astype(jnp.float32)[:, None]

    gate_act = contract_last(slot_rows, gate_piece)
    up_act = contract_last(slot_rows, up_piece)
    active, silu_slope = silu_parts(gate_act)
    hidden = (active * up_act).astype(jnp.bfloat16)
    partial_out = jnp.dot(hidden, down_piece, preferred_element_type=jnp.float32)
    scaled = (weight_wide * partial_out).astype(jnp.bfloat16)

    into_hidden = contract_last(slot_grads, down_piece)
    route_terms = jnp.sum(into_hidden * hidden.astype(jnp.float32), axis=1).astype(jnp.bfloat16)
    hidden_grad = weight_wide * into_hidden
    gate_grad = (hidden_grad * up_act * silu_slope).astype(jnp.bfloat16)
    up_grad = (hidden_grad * active).astype(jnp.bfloat16)
    row_grad = (
        jnp.dot(gate_grad, gate_piece, preferred_element_type=jnp.float32)
        + jnp.dot(up_grad, up_piece, preferred_element_type=jnp.float32)
    ).astype(jnp.bfloat16)
    scaled_grad = (weight_wide * slot_grads.astype(jnp.float32)).astype(jnp.bfloat16)
    grad_gate = contract_first(gate_grad, slot_rows).astype(jnp.bfloat16)[None]
    grad_up = contract_first(up_grad, slot_rows).astype(jnp.bfloat16)[None]
    grad_down = contract_first(hidden, scaled_grad).astype(jnp.bfloat16)[None]

    back_buf = jnp.concatenate([scaled, row_grad, column_block(route_terms, jnp.bfloat16)], axis=1)
    back = lax.all_to_all(
        back_buf.reshape(data_size, capacity, 2 * feature_width + PAD),
        "dp",
        split_axis=0,
        concat_axis=0,
        tiled=True,
    ).reshape(-1, 2 * feature_width + PAD)

    wide_token = spread(token_of).reshape(-1)
    wide_live = spread(slot_live).reshape(-1)
    wide_row = spread(row_of).reshape(-1)
    token_place = (
        (wide_token[None, :] == jnp.arange(tok_local, dtype=jnp.int32)[:, None])
        & (wide_live[None, :] > 0)
    ).astype(jnp.bfloat16)
    both_sum = jnp.dot(
        token_place, back[:, : 2 * feature_width], preferred_element_type=jnp.float32
    )
    row_place = (
        (wide_row[None, :] == jnp.arange(row_count, dtype=jnp.int32)[:, None])
        & (wide_live[None, :] > 0)
    ).astype(jnp.bfloat16)
    route_sum = jnp.dot(
        row_place, back[:, 2 * feature_width], preferred_element_type=jnp.float32
    )
    planes = jnp.transpose(
        both_sum.reshape(tok_local, 2, groups, part_width), (0, 2, 1, 3)
    ).reshape(tok_local, groups, 2 * part_width)
    route_row = jnp.pad(route_sum.reshape(groups, -1), ((0, 0), (0, 2 * part_width - row_count // groups)))
    packed = jnp.concatenate([planes, route_row[None]], axis=0).reshape(tok_local + 1, -1)
    reduced = lax.psum_scatter(packed, "expert", scatter_dimension=1, tiled=True)
    mixed_part = reduced[:tok_local, :part_width]
    token_part = reduced[:tok_local, part_width:]
    route_part = reduced[tok_local, : row_count // groups].reshape(-1, topk_count)
    return (
        mixed_part.astype(jnp.bfloat16),
        token_part.astype(jnp.bfloat16),
        route_part,
        grad_gate,
        grad_up,
        grad_down,
    )


def solution(mesh):
    return jax.shard_map(
        on_device,
        mesh=mesh,
        in_specs=(
            P("dp", "expert"),
            P("dp", None),
            P("dp", None),
            P("expert", "dp", None),
            P("expert", "dp", None),
            P("expert", "dp", None),
            P("dp", "expert"),
        ),
        out_specs=(
            P("dp", "expert"),
            P("dp", "expert"),
            P(("dp", "expert"), None),
            P("expert", "dp", None),
            P("expert", "dp", None),
            P("expert", "dp", None),
        ),
        check_vma=False,
    )
```

```python
import jax
import jax.numpy as jnp
from jax import lax
from jax.sharding import Mesh, PartitionSpec as P

PIECES = 4
PAD = 128


def contract_last(left_side, right_side):
    return lax.dot_general(
        left_side, right_side, (((1,), (1,)), ((), ())), preferred_element_type=jnp.float32
    )


def contract_first(left_side, right_side):
    return lax.dot_general(
        left_side, right_side, (((0,), (0,)), ((), ())), preferred_element_type=jnp.float32
    )


def silu_parts(gate_act):
    sigmoid_val = jax.nn.sigmoid(gate_act)
    return (gate_act * sigmoid_val, sigmoid_val * (1.0 + gate_act * (1.0 - sigmoid_val)))


def column_block(values, dtype):
    lane = jnp.arange(PAD, dtype=jnp.int32)[None, :] == 0
    return jnp.where(lane, values.astype(dtype)[:, None], jnp.zeros((), dtype))


def on_device(tokens, route_weight, expert_ids, gate_weight, up_weight, down_weight, grad_output):
    groups = lax.axis_size("expert")
    group_index = lax.axis_index("expert")
    chips = lax.axis_size("dpc")
    cores = lax.axis_size("core")
    data_size = chips * cores
    exp_local = data_size // PIECES
    chip_share = chips // exp_local
    tok_local, topk_count = expert_ids.shape
    capacity = min(tok_local, 2 * tok_local * topk_count // (exp_local * groups))
    part_width = tokens.shape[1]
    both = jnp.concatenate([tokens, grad_output], axis=1)
    gathered = lax.all_gather(both, "expert", axis=0, tiled=False)
    gathered = gathered.reshape(groups, tok_local, 2, part_width)
    full_both = jnp.transpose(gathered, (1, 2, 0, 3)).reshape(tok_local, 2 * groups * part_width)
    feature_width = groups * part_width
    row_width = 2 * feature_width + PAD
    gate_piece = gate_weight[0]
    up_piece = up_weight[0]
    down_piece = down_weight[0]
    flat_ids = expert_ids.reshape(-1)
    row_count = flat_ids.shape[0]
    owned_rows = flat_ids // exp_local == group_index
    local_ids = flat_ids % exp_local
    chosen = (
        (local_ids[:, None] == jnp.arange(exp_local, dtype=jnp.int32)[None, :])
        & owned_rows[:, None]
    ).astype(jnp.int32)
    slot_ranks = jnp.sum(chosen * (jnp.cumsum(chosen, axis=0) - 1), axis=1)
    slot_count = exp_local * capacity
    slot_pos = jnp.where(owned_rows, local_ids * capacity + slot_ranks, slot_count)
    row_index = jnp.arange(row_count, dtype=jnp.int32)
    row_of = jnp.zeros((slot_count,), jnp.int32).at[slot_pos].set(row_index, mode="drop")
    slot_live = (
        jnp.zeros((slot_count,), jnp.int32).at[slot_pos].set(jnp.ones_like(row_index), mode="drop")
    )
    token_of = row_of // topk_count
    keep_mask = slot_live.astype(tokens.dtype)[:, None]
    slot_weight = route_weight.reshape(-1)[row_of] * slot_live.astype(route_weight.dtype)

    def spread(values):
        trailing = values.shape[1:]
        grouped = values.reshape((exp_local, 1, capacity) + trailing)
        return jnp.broadcast_to(grouped, (exp_local, chip_share, capacity) + trailing).reshape(
            (chips, capacity) + trailing
        )

    send_buf = jnp.concatenate(
        [full_both[token_of] * keep_mask, column_block(slot_weight, tokens.dtype)], axis=1
    )
    half_buf = lax.all_to_all(spread(send_buf), "dpc", split_axis=0, concat_axis=0, tiled=True)
    recv_buf = lax.all_to_all(
        jnp.broadcast_to(half_buf[None], (cores,) + half_buf.shape),
        "core",
        split_axis=0,
        concat_axis=0,
        tiled=True,
    ).reshape(-1, row_width)
    slot_rows = recv_buf[:, :feature_width]
    slot_grads = recv_buf[:, feature_width : 2 * feature_width]
    slot_scale = recv_buf[:, 2 * feature_width]
    weight_wide = slot_scale.astype(jnp.float32)[:, None]

    gate_act = contract_last(slot_rows, gate_piece)
    up_act = contract_last(slot_rows, up_piece)
    active, silu_slope = silu_parts(gate_act)
    hidden = (active * up_act).astype(jnp.bfloat16)
    partial_out = jnp.dot(hidden, down_piece, preferred_element_type=jnp.float32)
    scaled = (weight_wide * partial_out).astype(jnp.bfloat16)

    into_hidden = contract_last(slot_grads, down_piece)
    route_terms = jnp.sum(into_hidden * hidden.astype(jnp.float32), axis=1).astype(jnp.bfloat16)
    hidden_grad = weight_wide * into_hidden
    gate_grad = (hidden_grad * up_act * silu_slope).astype(jnp.bfloat16)
    up_grad = (hidden_grad * active).astype(jnp.bfloat16)
    row_grad = (
        jnp.dot(gate_grad, gate_piece, preferred_element_type=jnp.float32)
        + jnp.dot(up_grad, up_piece, preferred_element_type=jnp.float32)
    ).astype(jnp.bfloat16)
    scaled_grad = (weight_wide * slot_grads.astype(jnp.float32)).astype(jnp.bfloat16)
    grad_gate = contract_first(gate_grad, slot_rows).astype(jnp.bfloat16)[None]
    grad_up = contract_first(up_grad, slot_rows).astype(jnp.bfloat16)[None]
    grad_down = contract_first(hidden, scaled_grad).astype(jnp.bfloat16)[None]

    core_index = lax.axis_index("core")
    piece_buf = jnp.concatenate([scaled, row_grad], axis=1).reshape(cores, -1, 2 * feature_width)
    pair = lax.all_to_all(piece_buf, "core", split_axis=0, concat_axis=0, tiled=True)
    pair_terms = lax.all_to_all(
        route_terms.reshape(cores, -1), "core", split_axis=0, concat_axis=0, tiled=True
    )
    pair_sum = jnp.sum(pair.astype(jnp.float32), axis=0).astype(jnp.bfloat16)
    lane = jnp.arange(PAD, dtype=jnp.int32)[None, :]
    term_block = jnp.zeros((pair_terms.shape[1], PAD), jnp.bfloat16)
    for k in range(cores):
        term_block = jnp.where(lane == k, pair_terms[k][:, None], term_block)
    back_buf = jnp.concatenate([pair_sum, term_block], axis=1)
    back = lax.all_to_all(
        back_buf.reshape(chips, capacity, row_width),
        "dpc",
        split_axis=0,
        concat_axis=0,
        tiled=True,
    ).reshape(-1, row_width)

    wide_token = spread(token_of).reshape(-1)
    wide_live = spread(slot_live).reshape(-1)
    wide_row = spread(row_of).reshape(-1)
    token_place = (
        (wide_token[None, :] == jnp.arange(tok_local, dtype=jnp.int32)[:, None])
        & (wide_live[None, :] > 0)
    ).astype(jnp.bfloat16)
    both_sum = jnp.dot(
        token_place, back[:, : 2 * feature_width], preferred_element_type=jnp.float32
    )
    row_place = (
        (wide_row[None, :] == jnp.arange(row_count, dtype=jnp.int32)[:, None])
        & (wide_live[None, :] > 0)
    ).astype(jnp.bfloat16)
    route_sum = jnp.dot(
        row_place,
        back[:, 2 * feature_width : 2 * feature_width + cores],
        preferred_element_type=jnp.float32,
    ).sum(axis=1)
    planes = jnp.transpose(
        both_sum.reshape(tok_local, 2, groups, part_width), (0, 2, 1, 3)
    ).reshape(tok_local, groups, 2 * part_width)
    route_row = jnp.pad(route_sum.reshape(groups, -1), ((0, 0), (0, 2 * part_width - row_count // groups)))
    packed = jnp.concatenate([planes, route_row[None]], axis=0).reshape(tok_local + 1, -1)
    reduced = lax.psum_scatter(packed, "expert", scatter_dimension=1, tiled=True)
    mixed_part = reduced[:tok_local, :part_width]
    token_part = reduced[:tok_local, part_width:]
    route_part = reduced[tok_local, : row_count // groups].reshape(-1, topk_count)
    return (
        mixed_part.astype(jnp.bfloat16),
        token_part.astype(jnp.bfloat16),
        route_part,
        grad_gate,
        grad_up,
        grad_down,
    )


def solution(mesh):
    devices = mesh.devices
    data_size, groups = devices.shape
    chip_mesh = Mesh(devices.reshape(data_size // 2, 2, groups), ("dpc", "core", "expert"))
    dp = ("dpc", "core")
    return jax.shard_map(
        on_device,
        mesh=chip_mesh,
        in_specs=(
            P(dp, "expert"),
            P(dp, None),
            P(dp, None),
            P("expert", dp, None),
            P("expert", dp, None),
            P("expert", dp, None),
            P(dp, "expert"),
        ),
        out_specs=(
            P(dp, "expert"),
            P(dp, "expert"),
            P(("dpc", "core", "expert"), None),
            P("expert", dp, None),
            P("expert", dp, None),
            P("expert", dp, None),
        ),
        check_vma=False,
    )
```

```python
import jax
import jax.numpy as jnp
from jax import lax
from jax.sharding import Mesh, PartitionSpec as P

PIECES = 4
PAD = 128


def contract_last(left_side, right_side):
    return lax.dot_general(
        left_side, right_side, (((1,), (1,)), ((), ())), preferred_element_type=jnp.float32
    )


def contract_first(left_side, right_side):
    return lax.dot_general(
        left_side, right_side, (((0,), (0,)), ((), ())), preferred_element_type=jnp.float32
    )


def silu_parts(gate_act):
    sigmoid_val = jax.nn.sigmoid(gate_act)
    return (gate_act * sigmoid_val, sigmoid_val * (1.0 + gate_act * (1.0 - sigmoid_val)))


def column_block(values, dtype):
    lane = jnp.arange(PAD, dtype=jnp.int32)[None, :] == 0
    return jnp.where(lane, values.astype(dtype)[:, None], jnp.zeros((), dtype))


def on_device(tokens, route_weight, expert_ids, gate_weight, up_weight, down_weight, grad_output):
    groups = lax.axis_size("expert")
    group_index = lax.axis_index("expert")
    chips = lax.axis_size("dpc")
    cores = lax.axis_size("core")
    data_size = chips * cores
    exp_local = data_size // PIECES
    chip_share = chips // exp_local
    tok_local, topk_count = expert_ids.shape
    capacity = min(tok_local, 2 * tok_local * topk_count // (exp_local * groups))
    part_width = tokens.shape[1]
    both = jnp.concatenate([tokens, grad_output], axis=1)
    gathered = lax.all_to_all(
        jnp.broadcast_to(both[None], (groups,) + both.shape),
        "expert",
        split_axis=0,
        concat_axis=0,
        tiled=True,
    )
    gathered = gathered.reshape(groups, tok_local, 2, part_width)
    full_both = jnp.transpose(gathered, (1, 2, 0, 3)).reshape(tok_local, 2 * groups * part_width)
    feature_width = groups * part_width
    row_width = 2 * feature_width + PAD
    gate_piece = gate_weight[0]
    up_piece = up_weight[0]
    down_piece = down_weight[0]
    flat_ids = expert_ids.reshape(-1)
    row_count = flat_ids.shape[0]
    owned_rows = flat_ids // exp_local == group_index
    local_ids = flat_ids % exp_local
    chosen = (
        (local_ids[:, None] == jnp.arange(exp_local, dtype=jnp.int32)[None, :])
        & owned_rows[:, None]
    ).astype(jnp.int32)
    slot_ranks = jnp.sum(chosen * (jnp.cumsum(chosen, axis=0) - 1), axis=1)
    slot_count = exp_local * capacity
    slot_pos = jnp.where(owned_rows, local_ids * capacity + slot_ranks, slot_count)
    row_index = jnp.arange(row_count, dtype=jnp.int32)
    row_of = jnp.zeros((slot_count,), jnp.int32).at[slot_pos].set(row_index, mode="drop")
    slot_live = (
        jnp.zeros((slot_count,), jnp.int32).at[slot_pos].set(jnp.ones_like(row_index), mode="drop")
    )
    token_of = row_of // topk_count
    keep_mask = slot_live.astype(tokens.dtype)[:, None]
    slot_weight = route_weight.reshape(-1)[row_of] * slot_live.astype(route_weight.dtype)

    def spread(values):
        trailing = values.shape[1:]
        grouped = values.reshape((exp_local, 1, capacity) + trailing)
        return jnp.broadcast_to(grouped, (exp_local, chip_share, capacity) + trailing).reshape(
            (chips, capacity) + trailing
        )

    send_buf = jnp.concatenate(
        [full_both[token_of] * keep_mask, column_block(slot_weight, tokens.dtype)], axis=1
    )
    half_buf = lax.all_to_all(spread(send_buf), "dpc", split_axis=0, concat_axis=0, tiled=True)
    recv_buf = lax.all_to_all(
        jnp.broadcast_to(half_buf[None], (cores,) + half_buf.shape),
        "core",
        split_axis=0,
        concat_axis=0,
        tiled=True,
    ).reshape(-1, row_width)
    slot_rows = recv_buf[:, :feature_width]
    slot_grads = recv_buf[:, feature_width : 2 * feature_width]
    slot_scale = recv_buf[:, 2 * feature_width]
    weight_wide = slot_scale.astype(jnp.float32)[:, None]

    gate_act = contract_last(slot_rows, gate_piece)
    up_act = contract_last(slot_rows, up_piece)
    active, silu_slope = silu_parts(gate_act)
    hidden = (active * up_act).astype(jnp.bfloat16)
    partial_out = jnp.dot(hidden, down_piece, preferred_element_type=jnp.float32)
    scaled = (weight_wide * partial_out).astype(jnp.bfloat16)

    into_hidden = contract_last(slot_grads, down_piece)
    route_terms = jnp.sum(into_hidden * hidden.astype(jnp.float32), axis=1).astype(jnp.bfloat16)
    hidden_grad = weight_wide * into_hidden
    gate_grad = (hidden_grad * up_act * silu_slope).astype(jnp.bfloat16)
    up_grad = (hidden_grad * active).astype(jnp.bfloat16)
    row_grad = (
        jnp.dot(gate_grad, gate_piece, preferred_element_type=jnp.float32)
        + jnp.dot(up_grad, up_piece, preferred_element_type=jnp.float32)
    ).astype(jnp.bfloat16)
    scaled_grad = (weight_wide * slot_grads.astype(jnp.float32)).astype(jnp.bfloat16)
    grad_gate = contract_first(gate_grad, slot_rows).astype(jnp.bfloat16)[None]
    grad_up = contract_first(up_grad, slot_rows).astype(jnp.bfloat16)[None]
    grad_down = contract_first(hidden, scaled_grad).astype(jnp.bfloat16)[None]

    core_index = lax.axis_index("core")
    piece_buf = jnp.concatenate([scaled, row_grad], axis=1).reshape(cores, -1, 2 * feature_width)
    pair = lax.all_to_all(piece_buf, "core", split_axis=0, concat_axis=0, tiled=True)
    pair_terms = lax.all_to_all(
        route_terms.reshape(cores, -1), "core", split_axis=0, concat_axis=0, tiled=True
    )
    pair_sum = jnp.sum(pair.astype(jnp.float32), axis=0).astype(jnp.bfloat16)
    lane = jnp.arange(PAD, dtype=jnp.int32)[None, :]
    term_block = jnp.zeros((pair_terms.shape[1], PAD), jnp.bfloat16)
    for k in range(cores):
        term_block = jnp.where(lane == k, pair_terms[k][:, None], term_block)
    back_buf = jnp.concatenate([pair_sum, term_block], axis=1)
    back = lax.all_to_all(
        back_buf.reshape(chips, capacity, row_width),
        "dpc",
        split_axis=0,
        concat_axis=0,
        tiled=True,
    ).reshape(-1, row_width)

    wide_token = spread(token_of).reshape(-1)
    wide_live = spread(slot_live).reshape(-1)
    wide_row = spread(row_of).reshape(-1)
    token_place = (
        (wide_token[None, :] == jnp.arange(tok_local, dtype=jnp.int32)[:, None])
        & (wide_live[None, :] > 0)
    ).astype(jnp.bfloat16)
    both_sum = jnp.dot(
        token_place, back[:, : 2 * feature_width], preferred_element_type=jnp.float32
    )
    row_place = (
        (wide_row[None, :] == jnp.arange(row_count, dtype=jnp.int32)[:, None])
        & (wide_live[None, :] > 0)
    ).astype(jnp.bfloat16)
    route_sum = jnp.dot(
        row_place,
        back[:, 2 * feature_width : 2 * feature_width + cores],
        preferred_element_type=jnp.float32,
    ).sum(axis=1)
    planes = jnp.transpose(
        both_sum.reshape(tok_local, 2, groups, part_width), (0, 2, 1, 3)
    ).reshape(tok_local, groups, 2 * part_width)
    route_row = jnp.pad(route_sum.reshape(groups, -1), ((0, 0), (0, 2 * part_width - row_count // groups)))
    packed = jnp.concatenate([planes, route_row[None]], axis=0).reshape(tok_local + 1, -1)
    reduced = lax.psum_scatter(packed, "expert", scatter_dimension=1, tiled=True)
    mixed_part = reduced[:tok_local, :part_width]
    token_part = reduced[:tok_local, part_width:]
    route_part = reduced[tok_local, : row_count // groups].reshape(-1, topk_count)
    return (
        mixed_part.astype(jnp.bfloat16),
        token_part.astype(jnp.bfloat16),
        route_part,
        grad_gate,
        grad_up,
        grad_down,
    )


def solution(mesh):
    devices = mesh.devices
    data_size, groups = devices.shape
    chip_mesh = Mesh(devices.reshape(data_size // 2, 2, groups), ("dpc", "core", "expert"))
    dp = ("dpc", "core")
    return jax.shard_map(
        on_device,
        mesh=chip_mesh,
        in_specs=(
            P(dp, "expert"),
            P(dp, None),
            P(dp, None),
            P("expert", dp, None),
            P("expert", dp, None),
            P("expert", dp, None),
            P(dp, "expert"),
        ),
        out_specs=(
            P(dp, "expert"),
            P(dp, "expert"),
            P(("dpc", "core", "expert"), None),
            P("expert", dp, None),
            P("expert", dp, None),
            P("expert", dp, None),
        ),
        check_vma=False,
    )
```

```python
import jax
import jax.numpy as jnp
from jax import lax
from jax.sharding import Mesh, PartitionSpec as P

PIECES = 4
PAD = 128


def contract_last(left_side, right_side):
    return lax.dot_general(
        left_side, right_side, (((1,), (1,)), ((), ())), preferred_element_type=jnp.float32
    )


def contract_first(left_side, right_side):
    return lax.dot_general(
        left_side, right_side, (((0,), (0,)), ((), ())), preferred_element_type=jnp.float32
    )


def silu_parts(gate_act):
    sigmoid_val = jax.nn.sigmoid(gate_act)
    return (gate_act * sigmoid_val, sigmoid_val * (1.0 + gate_act * (1.0 - sigmoid_val)))


def column_block(values, dtype):
    lane = jnp.arange(PAD, dtype=jnp.int32)[None, :] == 0
    return jnp.where(lane, values.astype(dtype)[:, None], jnp.zeros((), dtype))


def on_device(tokens, route_weight, expert_ids, gate_weight, up_weight, down_weight, grad_output):
    groups = lax.axis_size("expert")
    group_index = lax.axis_index("expert")
    chips = lax.axis_size("dpc")
    cores = lax.axis_size("core")
    data_size = chips * cores
    exp_local = data_size // PIECES
    chip_share = chips // exp_local
    tok_local, topk_count = expert_ids.shape
    capacity = min(tok_local, 2 * tok_local * topk_count // (exp_local * groups))
    part_width = tokens.shape[1]
    both = jnp.concatenate([tokens, grad_output], axis=1)
    gathered = lax.all_to_all(
        jnp.broadcast_to(both[None], (groups,) + both.shape),
        "expert",
        split_axis=0,
        concat_axis=0,
        tiled=True,
    )
    gathered = gathered.reshape(groups, tok_local, 2, part_width)
    full_both = jnp.transpose(gathered, (1, 2, 0, 3)).reshape(tok_local, 2 * groups * part_width)
    feature_width = groups * part_width
    row_width = 2 * feature_width + PAD
    gate_piece = gate_weight[0]
    up_piece = up_weight[0]
    down_piece = down_weight[0]
    flat_ids = expert_ids.reshape(-1)
    row_count = flat_ids.shape[0]
    owned_rows = flat_ids // exp_local == group_index
    local_ids = flat_ids % exp_local
    chosen = (
        (local_ids[:, None] == jnp.arange(exp_local, dtype=jnp.int32)[None, :])
        & owned_rows[:, None]
    ).astype(jnp.int32)
    slot_ranks = jnp.sum(chosen * (jnp.cumsum(chosen, axis=0) - 1), axis=1)
    slot_count = exp_local * capacity
    slot_pos = jnp.where(owned_rows, local_ids * capacity + slot_ranks, slot_count)
    row_index = jnp.arange(row_count, dtype=jnp.int32)
    row_of = jnp.zeros((slot_count,), jnp.int32).at[slot_pos].set(row_index, mode="drop")
    slot_live = (
        jnp.zeros((slot_count,), jnp.int32).at[slot_pos].set(jnp.ones_like(row_index), mode="drop")
    )
    token_of = row_of // topk_count
    keep_mask = slot_live.astype(tokens.dtype)[:, None]
    slot_weight = route_weight.reshape(-1)[row_of] * slot_live.astype(route_weight.dtype)

    def spread(values):
        trailing = values.shape[1:]
        grouped = values.reshape((exp_local, 1, capacity) + trailing)
        return jnp.broadcast_to(grouped, (exp_local, chip_share, capacity) + trailing).reshape(
            (chips, capacity) + trailing
        )

    send_buf = jnp.concatenate(
        [full_both[token_of] * keep_mask, column_block(slot_weight, tokens.dtype)], axis=1
    )
    half_buf = lax.all_to_all(spread(send_buf), "dpc", split_axis=0, concat_axis=0, tiled=True)
    recv_buf = lax.all_to_all(
        jnp.broadcast_to(half_buf[None], (cores,) + half_buf.shape),
        "core",
        split_axis=0,
        concat_axis=0,
        tiled=True,
    ).reshape(-1, row_width)
    slot_rows = recv_buf[:, :feature_width]
    slot_grads = recv_buf[:, feature_width : 2 * feature_width]
    slot_scale = recv_buf[:, 2 * feature_width]
    weight_wide = slot_scale.astype(jnp.float32)[:, None]

    gate_act = contract_last(slot_rows, gate_piece)
    up_act = contract_last(slot_rows, up_piece)
    active, silu_slope = silu_parts(gate_act)
    hidden = (active * up_act).astype(jnp.bfloat16)
    partial_out = jnp.dot(hidden, down_piece, preferred_element_type=jnp.float32)
    scaled = (weight_wide * partial_out).astype(jnp.bfloat16)

    into_hidden = contract_last(slot_grads, down_piece)
    route_terms = jnp.sum(into_hidden * hidden.astype(jnp.float32), axis=1).astype(jnp.bfloat16)
    hidden_grad = weight_wide * into_hidden
    gate_grad = (hidden_grad * up_act * silu_slope).astype(jnp.bfloat16)
    up_grad = (hidden_grad * active).astype(jnp.bfloat16)
    row_grad = (
        jnp.dot(gate_grad, gate_piece, preferred_element_type=jnp.float32)
        + jnp.dot(up_grad, up_piece, preferred_element_type=jnp.float32)
    ).astype(jnp.bfloat16)
    scaled_grad = (weight_wide * slot_grads.astype(jnp.float32)).astype(jnp.bfloat16)
    grad_gate = contract_first(gate_grad, slot_rows).astype(jnp.bfloat16)[None]
    grad_up = contract_first(up_grad, slot_rows).astype(jnp.bfloat16)[None]
    grad_down = contract_first(hidden, scaled_grad).astype(jnp.bfloat16)[None]

    core_index = lax.axis_index("core")
    piece_buf = jnp.concatenate([scaled, row_grad], axis=1).reshape(cores, -1, 2 * feature_width)
    pair = lax.all_to_all(piece_buf, "core", split_axis=0, concat_axis=0, tiled=True)
    pair_terms = lax.all_to_all(
        route_terms.reshape(cores, -1), "core", split_axis=0, concat_axis=0, tiled=True
    )
    pair_sum = jnp.sum(pair.astype(jnp.float32), axis=0).astype(jnp.bfloat16)
    lane = jnp.arange(PAD, dtype=jnp.int32)[None, :]
    term_block = jnp.zeros((pair_terms.shape[1], PAD), jnp.bfloat16)
    for k in range(cores):
        term_block = jnp.where(lane == k, pair_terms[k][:, None], term_block)
    back_buf = jnp.concatenate([pair_sum, term_block], axis=1)
    back = lax.all_to_all(
        back_buf.reshape(chips, capacity, row_width),
        "dpc",
        split_axis=0,
        concat_axis=0,
        tiled=True,
    ).reshape(-1, row_width)

    wide_token = spread(token_of).reshape(-1)
    wide_live = spread(slot_live).reshape(-1)
    wide_row = spread(row_of).reshape(-1)
    token_place = (
        (wide_token[None, :] == jnp.arange(tok_local, dtype=jnp.int32)[:, None])
        & (wide_live[None, :] > 0)
    ).astype(jnp.bfloat16)
    both_sum = jnp.dot(
        token_place, back[:, : 2 * feature_width], preferred_element_type=jnp.float32
    )
    row_place = (
        (wide_row[None, :] == jnp.arange(row_count, dtype=jnp.int32)[:, None])
        & (wide_live[None, :] > 0)
    ).astype(jnp.bfloat16)
    route_sum = jnp.dot(
        row_place,
        back[:, 2 * feature_width : 2 * feature_width + cores],
        preferred_element_type=jnp.float32,
    ).sum(axis=1)
    planes = jnp.transpose(
        both_sum.reshape(tok_local, 2, groups, part_width), (2, 0, 1, 3)
    ).reshape(groups, tok_local, 2 * part_width)
    route_row = jnp.pad(route_sum.reshape(groups, -1), ((0, 0), (0, 2 * part_width - row_count // groups)))
    packed = jnp.concatenate([planes, route_row[:, None]], axis=1).astype(jnp.bfloat16)
    received = lax.all_to_all(packed, "expert", split_axis=0, concat_axis=0, tiled=True)
    reduced = jnp.sum(received.astype(jnp.float32), axis=0)
    mixed_part = reduced[:tok_local, :part_width]
    token_part = reduced[:tok_local, part_width:]
    route_part = reduced[tok_local, : row_count // groups].reshape(-1, topk_count)
    return (
        mixed_part.astype(jnp.bfloat16),
        token_part.astype(jnp.bfloat16),
        route_part,
        grad_gate,
        grad_up,
        grad_down,
    )


def solution(mesh):
    devices = mesh.devices
    data_size, groups = devices.shape
    chip_mesh = Mesh(devices.reshape(data_size // 2, 2, groups), ("dpc", "core", "expert"))
    dp = ("dpc", "core")
    return jax.shard_map(
        on_device,
        mesh=chip_mesh,
        in_specs=(
            P(dp, "expert"),
            P(dp, None),
            P(dp, None),
            P("expert", dp, None),
            P("expert", dp, None),
            P("expert", dp, None),
            P(dp, "expert"),
        ),
        out_specs=(
            P(dp, "expert"),
            P(dp, "expert"),
            P(("dpc", "core", "expert"), None),
            P("expert", dp, None),
            P("expert", dp, None),
            P("expert", dp, None),
        ),
        check_vma=False,
    )
```

```python
import jax
import jax.numpy as jnp
from jax import lax
from jax.sharding import Mesh, PartitionSpec as P

PIECES = 4
PAD = 128


def contract_last(left_side, right_side):
    return lax.dot_general(
        left_side, right_side, (((1,), (1,)), ((), ())), preferred_element_type=jnp.float32
    )


def contract_first(left_side, right_side):
    return lax.dot_general(
        left_side, right_side, (((0,), (0,)), ((), ())), preferred_element_type=jnp.float32
    )


def silu_parts(gate_act):
    sigmoid_val = jax.nn.sigmoid(gate_act)
    return (gate_act * sigmoid_val, sigmoid_val * (1.0 + gate_act * (1.0 - sigmoid_val)))


def column_block(values, dtype):
    lane = jnp.arange(PAD, dtype=jnp.int32)[None, :] == 0
    return jnp.where(lane, values.astype(dtype)[:, None], jnp.zeros((), dtype))


def on_device(tokens, route_weight, expert_ids, gate_weight, up_weight, down_weight, grad_output):
    groups = lax.axis_size("expert")
    group_index = lax.axis_index("expert")
    chips = lax.axis_size("dpc")
    cores = lax.axis_size("core")
    data_size = chips * cores
    exp_local = data_size // PIECES
    chip_share = chips // exp_local
    tok_local, topk_count = expert_ids.shape
    capacity = min(tok_local, 2 * tok_local * topk_count // (exp_local * groups))
    part_width = tokens.shape[1]
    feature_width = groups * part_width

    def gather_features(block):
        spread_out = jnp.broadcast_to(block[None], (groups,) + block.shape)
        got = lax.all_to_all(spread_out, "expert", split_axis=0, concat_axis=0, tiled=True)
        return jnp.transpose(got, (1, 0, 2)).reshape(tok_local, feature_width)

    full_x = gather_features(tokens)
    full_dy = gather_features(grad_output)
    gate_piece = gate_weight[0]
    up_piece = up_weight[0]
    down_piece = down_weight[0]
    flat_ids = expert_ids.reshape(-1)
    row_count = flat_ids.shape[0]
    owned_rows = flat_ids // exp_local == group_index
    local_ids = flat_ids % exp_local
    chosen = (
        (local_ids[:, None] == jnp.arange(exp_local, dtype=jnp.int32)[None, :])
        & owned_rows[:, None]
    ).astype(jnp.int32)
    slot_ranks = jnp.sum(chosen * (jnp.cumsum(chosen, axis=0) - 1), axis=1)
    slot_count = exp_local * capacity
    slot_pos = jnp.where(owned_rows, local_ids * capacity + slot_ranks, slot_count)
    row_index = jnp.arange(row_count, dtype=jnp.int32)
    row_of = jnp.zeros((slot_count,), jnp.int32).at[slot_pos].set(row_index, mode="drop")
    slot_live = (
        jnp.zeros((slot_count,), jnp.int32).at[slot_pos].set(jnp.ones_like(row_index), mode="drop")
    )
    token_of = row_of // topk_count
    keep_mask = slot_live.astype(tokens.dtype)[:, None]
    slot_weight = route_weight.reshape(-1)[row_of] * slot_live.astype(route_weight.dtype)

    def spread(values):
        trailing = values.shape[1:]
        grouped = values.reshape((exp_local, 1, capacity) + trailing)
        return jnp.broadcast_to(grouped, (exp_local, chip_share, capacity) + trailing).reshape(
            (chips, capacity) + trailing
        )

    def dispatch(send_buf):
        width = send_buf.shape[1]
        half_buf = lax.all_to_all(spread(send_buf), "dpc", split_axis=0, concat_axis=0, tiled=True)
        return lax.all_to_all(
            jnp.broadcast_to(half_buf[None], (cores,) + half_buf.shape),
            "core",
            split_axis=0,
            concat_axis=0,
            tiled=True,
        ).reshape(-1, width)

    def pair_sum(values):
        pair = lax.all_to_all(
            values.reshape((cores, -1) + values.shape[1:]), "core", split_axis=0, concat_axis=0, tiled=True
        )
        return jnp.sum(pair.astype(jnp.float32), axis=0).astype(jnp.bfloat16)

    def send_back(values):
        width = values.shape[1]
        return lax.all_to_all(
            values.reshape(chips, capacity, width), "dpc", split_axis=0, concat_axis=0, tiled=True
        ).reshape(-1, width)

    wide_token = spread(token_of).reshape(-1)
    wide_live = spread(slot_live).reshape(-1)
    wide_row = spread(row_of).reshape(-1)
    token_place = (
        (wide_token[None, :] == jnp.arange(tok_local, dtype=jnp.int32)[:, None])
        & (wide_live[None, :] > 0)
    ).astype(jnp.bfloat16)

    def combine(rows, extra):
        total = jnp.dot(token_place, rows, preferred_element_type=jnp.float32)
        planes = jnp.transpose(total.reshape(tok_local, groups, part_width), (1, 0, 2))
        if extra is not None:
            planes = jnp.concatenate([planes, extra[:, None]], axis=1)
        received = lax.all_to_all(
            planes.astype(jnp.bfloat16), "expert", split_axis=0, concat_axis=0, tiled=True
        )
        return jnp.sum(received.astype(jnp.float32), axis=0)

    recv_x = dispatch(
        jnp.concatenate([full_x[token_of] * keep_mask, column_block(slot_weight, tokens.dtype)], axis=1)
    )
    slot_rows = recv_x[:, :feature_width]
    slot_scale = recv_x[:, feature_width]
    weight_wide = slot_scale.astype(jnp.float32)[:, None]
    gate_act = contract_last(slot_rows, gate_piece)
    up_act = contract_last(slot_rows, up_piece)
    active, silu_slope = silu_parts(gate_act)
    hidden = (active * up_act).astype(jnp.bfloat16)
    partial_out = jnp.dot(hidden, down_piece, preferred_element_type=jnp.float32)
    scaled = (weight_wide * partial_out).astype(jnp.bfloat16)
    mixed_part = combine(send_back(pair_sum(scaled)), None)

    slot_grads = dispatch(full_dy[token_of] * keep_mask)
    into_hidden = contract_last(slot_grads, down_piece)
    route_terms = jnp.sum(into_hidden * hidden.astype(jnp.float32), axis=1).astype(jnp.bfloat16)
    hidden_grad = weight_wide * into_hidden
    gate_grad = (hidden_grad * up_act * silu_slope).astype(jnp.bfloat16)
    up_grad = (hidden_grad * active).astype(jnp.bfloat16)
    row_grad = (
        jnp.dot(gate_grad, gate_piece, preferred_element_type=jnp.float32)
        + jnp.dot(up_grad, up_piece, preferred_element_type=jnp.float32)
    ).astype(jnp.bfloat16)
    scaled_grad = (weight_wide * slot_grads.astype(jnp.float32)).astype(jnp.bfloat16)
    grad_gate = contract_first(gate_grad, slot_rows).astype(jnp.bfloat16)[None]
    grad_up = contract_first(up_grad, slot_rows).astype(jnp.bfloat16)[None]
    grad_down = contract_first(hidden, scaled_grad).astype(jnp.bfloat16)[None]

    pair_terms = lax.all_to_all(
        route_terms.reshape(cores, -1), "core", split_axis=0, concat_axis=0, tiled=True
    )
    lane = jnp.arange(PAD, dtype=jnp.int32)[None, :]
    term_block = jnp.zeros((pair_terms.shape[1], PAD), jnp.bfloat16)
    for k in range(cores):
        term_block = jnp.where(lane == k, pair_terms[k][:, None], term_block)
    back = send_back(jnp.concatenate([pair_sum(row_grad), term_block], axis=1))
    row_place = (
        (wide_row[None, :] == jnp.arange(row_count, dtype=jnp.int32)[:, None])
        & (wide_live[None, :] > 0)
    ).astype(jnp.bfloat16)
    route_sum = jnp.dot(
        row_place,
        back[:, feature_width : feature_width + cores],
        preferred_element_type=jnp.float32,
    ).sum(axis=1)
    route_row = jnp.pad(route_sum.reshape(groups, -1), ((0, 0), (0, part_width - row_count // groups)))
    token_total = combine(back[:, :feature_width], route_row)
    token_part = token_total[:tok_local]
    route_part = token_total[tok_local, : row_count // groups].reshape(-1, topk_count)
    return (
        mixed_part.astype(jnp.bfloat16),
        token_part.astype(jnp.bfloat16),
        route_part,
        grad_gate,
        grad_up,
        grad_down,
    )


def solution(mesh):
    devices = mesh.devices
    data_size, groups = devices.shape
    chip_mesh = Mesh(devices.reshape(data_size // 2, 2, groups), ("dpc", "core", "expert"))
    dp = ("dpc", "core")
    return jax.shard_map(
        on_device,
        mesh=chip_mesh,
        in_specs=(
            P(dp, "expert"),
            P(dp, None),
            P(dp, None),
            P("expert", dp, None),
            P("expert", dp, None),
            P("expert", dp, None),
            P(dp, "expert"),
        ),
        out_specs=(
            P(dp, "expert"),
            P(dp, "expert"),
            P(("dpc", "core", "expert"), None),
            P("expert", dp, None),
            P("expert", dp, None),
            P("expert", dp, None),
        ),
        check_vma=False,
    )
```

```python
import jax
import jax.numpy as jnp
from jax import lax
from jax.sharding import Mesh, PartitionSpec as P

PIECES = 4
PAD = 128


def contract_last(left_side, right_side):
    return lax.dot_general(
        left_side, right_side, (((1,), (1,)), ((), ())), preferred_element_type=jnp.float32
    )


def contract_first(left_side, right_side):
    return lax.dot_general(
        left_side, right_side, (((0,), (0,)), ((), ())), preferred_element_type=jnp.float32
    )


def silu_parts(gate_act):
    sigmoid_val = jax.nn.sigmoid(gate_act)
    return (gate_act * sigmoid_val, sigmoid_val * (1.0 + gate_act * (1.0 - sigmoid_val)))


def column_block(values, dtype):
    lane = jnp.arange(PAD, dtype=jnp.int32)[None, :] == 0
    return jnp.where(lane, values.astype(dtype)[:, None], jnp.zeros((), dtype))


def on_device(tokens, route_weight, expert_ids, gate_weight, up_weight, down_weight, grad_output):
    groups = lax.axis_size("expert")
    group_index = lax.axis_index("expert")
    chips = lax.axis_size("dpc")
    cores = lax.axis_size("core")
    data_size = chips * cores
    exp_local = data_size // PIECES
    chip_share = chips // exp_local
    tok_local, topk_count = expert_ids.shape
    capacity = min(tok_local, 2 * tok_local * topk_count // (exp_local * groups))
    part_width = tokens.shape[1]
    both = jnp.concatenate([tokens, grad_output], axis=1)
    gathered = lax.all_to_all(
        jnp.broadcast_to(both[None], (groups,) + both.shape),
        "expert",
        split_axis=0,
        concat_axis=0,
        tiled=True,
    )
    gathered = gathered.reshape(groups, tok_local, 2, part_width)
    full_both = jnp.transpose(gathered, (1, 2, 0, 3)).reshape(tok_local, 2 * groups * part_width)
    feature_width = groups * part_width
    row_width = 2 * feature_width + PAD
    gate_piece = gate_weight[0]
    up_piece = up_weight[0]
    down_piece = down_weight[0]
    flat_ids = expert_ids.reshape(-1)
    row_count = flat_ids.shape[0]
    owned_rows = flat_ids // exp_local == group_index
    local_ids = flat_ids % exp_local
    chosen = (
        (local_ids[:, None] == jnp.arange(exp_local, dtype=jnp.int32)[None, :])
        & owned_rows[:, None]
    ).astype(jnp.int32)
    slot_ranks = jnp.sum(chosen * (jnp.cumsum(chosen, axis=0) - 1), axis=1)
    slot_count = exp_local * capacity
    slot_pos = jnp.where(owned_rows, local_ids * capacity + slot_ranks, slot_count)
    row_index = jnp.arange(row_count, dtype=jnp.int32)
    row_of = jnp.zeros((slot_count,), jnp.int32).at[slot_pos].set(row_index, mode="drop")
    slot_live = (
        jnp.zeros((slot_count,), jnp.int32).at[slot_pos].set(jnp.ones_like(row_index), mode="drop")
    )
    token_of = row_of // topk_count
    keep_mask = slot_live.astype(tokens.dtype)[:, None]
    slot_weight = route_weight.reshape(-1)[row_of] * slot_live.astype(route_weight.dtype)

    def spread(values):
        trailing = values.shape[1:]
        grouped = values.reshape((exp_local, 1, capacity) + trailing)
        return jnp.broadcast_to(grouped, (exp_local, chip_share, capacity) + trailing).reshape(
            (chips, capacity) + trailing
        )

    send_buf = jnp.concatenate(
        [full_both[token_of] * keep_mask, column_block(slot_weight, tokens.dtype)], axis=1
    )
    half_buf = lax.all_to_all(spread(send_buf), "dpc", split_axis=0, concat_axis=0, tiled=True)
    recv_buf = lax.all_to_all(
        jnp.broadcast_to(half_buf[None], (cores,) + half_buf.shape),
        "core",
        split_axis=0,
        concat_axis=0,
        tiled=True,
    ).reshape(-1, row_width)
    slot_rows = recv_buf[:, :feature_width]
    slot_grads = recv_buf[:, feature_width : 2 * feature_width]
    slot_scale = recv_buf[:, 2 * feature_width]
    weight_wide = slot_scale.astype(jnp.float32)[:, None]

    gate_act = contract_last(slot_rows, gate_piece)
    up_act = contract_last(slot_rows, up_piece)
    active, silu_slope = silu_parts(gate_act)
    hidden = (active * up_act).astype(jnp.bfloat16)
    partial_out = jnp.dot(hidden, down_piece, preferred_element_type=jnp.float32)
    scaled = (weight_wide * partial_out).astype(jnp.bfloat16)

    into_hidden = contract_last(slot_grads, down_piece)
    route_terms = jnp.sum(into_hidden * hidden.astype(jnp.float32), axis=1).astype(jnp.bfloat16)
    hidden_grad = weight_wide * into_hidden
    gate_grad = (hidden_grad * up_act * silu_slope).astype(jnp.bfloat16)
    up_grad = (hidden_grad * active).astype(jnp.bfloat16)
    row_grad = (
        jnp.dot(gate_grad, gate_piece, preferred_element_type=jnp.float32)
        + jnp.dot(up_grad, up_piece, preferred_element_type=jnp.float32)
    ).astype(jnp.bfloat16)
    scaled_grad = (weight_wide * slot_grads.astype(jnp.float32)).astype(jnp.bfloat16)
    grad_gate = contract_first(gate_grad, slot_rows).astype(jnp.bfloat16)[None]
    grad_up = contract_first(up_grad, slot_rows).astype(jnp.bfloat16)[None]
    grad_down = contract_first(hidden, scaled_grad).astype(jnp.bfloat16)[None]

    piece_buf = jnp.concatenate(
        [scaled, row_grad, column_block(route_terms, jnp.bfloat16)], axis=1
    ).reshape(cores, -1, row_width)
    pair = lax.all_to_all(piece_buf, "core", split_axis=0, concat_axis=0, tiled=True)
    pair_sum = jnp.sum(pair[:, :, : 2 * feature_width].astype(jnp.float32), axis=0).astype(jnp.bfloat16)
    lane = jnp.arange(PAD, dtype=jnp.int32)[None, :]
    term_block = jnp.zeros((pair.shape[1], PAD), jnp.bfloat16)
    for k in range(cores):
        term_block = jnp.where(lane == k, pair[k, :, 2 * feature_width : 2 * feature_width + 1], term_block)
    back_buf = jnp.concatenate([pair_sum, term_block], axis=1)
    back = lax.all_to_all(
        back_buf.reshape(chips, capacity, row_width),
        "dpc",
        split_axis=0,
        concat_axis=0,
        tiled=True,
    ).reshape(-1, row_width)

    wide_token = spread(token_of).reshape(-1)
    wide_live = spread(slot_live).reshape(-1)
    wide_row = spread(row_of).reshape(-1)
    token_place = (
        (wide_token[None, :] == jnp.arange(tok_local, dtype=jnp.int32)[:, None])
        & (wide_live[None, :] > 0)
    ).astype(jnp.bfloat16)
    both_sum = jnp.dot(
        token_place, back[:, : 2 * feature_width], preferred_element_type=jnp.float32
    )
    row_place = (
        (wide_row[None, :] == jnp.arange(row_count, dtype=jnp.int32)[:, None])
        & (wide_live[None, :] > 0)
    ).astype(jnp.bfloat16)
    route_sum = jnp.dot(
        row_place,
        back[:, 2 * feature_width : 2 * feature_width + cores],
        preferred_element_type=jnp.float32,
    ).sum(axis=1)
    planes = jnp.transpose(
        both_sum.reshape(tok_local, 2, groups, part_width), (2, 0, 1, 3)
    ).reshape(groups, tok_local, 2 * part_width)
    route_row = jnp.pad(route_sum.reshape(groups, -1), ((0, 0), (0, 2 * part_width - row_count // groups)))
    packed = jnp.concatenate([planes, route_row[:, None]], axis=1).astype(jnp.bfloat16)
    received = lax.all_to_all(packed, "expert", split_axis=0, concat_axis=0, tiled=True)
    reduced = jnp.sum(received.astype(jnp.float32), axis=0)
    mixed_part = reduced[:tok_local, :part_width]
    token_part = reduced[:tok_local, part_width:]
    route_part = reduced[tok_local, : row_count // groups].reshape(-1, topk_count)
    return (
        mixed_part.astype(jnp.bfloat16),
        token_part.astype(jnp.bfloat16),
        route_part,
        grad_gate,
        grad_up,
        grad_down,
    )


def solution(mesh):
    devices = mesh.devices
    data_size, groups = devices.shape
    chip_mesh = Mesh(devices.reshape(data_size // 2, 2, groups), ("dpc", "core", "expert"))
    dp = ("dpc", "core")
    return jax.shard_map(
        on_device,
        mesh=chip_mesh,
        in_specs=(
            P(dp, "expert"),
            P(dp, None),
            P(dp, None),
            P("expert", dp, None),
            P("expert", dp, None),
            P("expert", dp, None),
            P(dp, "expert"),
        ),
        out_specs=(
            P(dp, "expert"),
            P(dp, "expert"),
            P(("dpc", "core", "expert"), None),
            P("expert", dp, None),
            P("expert", dp, None),
            P("expert", dp, None),
        ),
        check_vma=False,
    )
```

```python
import jax
import jax.numpy as jnp
from jax import lax
from jax.sharding import Mesh, PartitionSpec as P

PIECES = 4
PAD = 128


def contract_last(left_side, right_side):
    return lax.dot_general(
        left_side, right_side, (((1,), (1,)), ((), ())), preferred_element_type=jnp.float32
    )


def contract_first(left_side, right_side):
    return lax.dot_general(
        left_side, right_side, (((0,), (0,)), ((), ())), preferred_element_type=jnp.float32
    )


def silu_parts(gate_act):
    sigmoid_val = jax.nn.sigmoid(gate_act)
    return (gate_act * sigmoid_val, sigmoid_val * (1.0 + gate_act * (1.0 - sigmoid_val)))


def column_block(values, dtype):
    lane = jnp.arange(PAD, dtype=jnp.int32)[None, :] == 0
    return jnp.where(lane, values.astype(dtype)[:, None], jnp.zeros((), dtype))


def on_device(tokens, route_weight, expert_ids, gate_weight, up_weight, down_weight, grad_output):
    groups = lax.axis_size("expert")
    group_index = lax.axis_index("expert")
    chips = lax.axis_size("dpc")
    cores = lax.axis_size("core")
    data_size = chips * cores
    exp_local = data_size // PIECES
    chip_share = chips // exp_local
    tok_local, topk_count = expert_ids.shape
    capacity = min(tok_local, 2 * tok_local * topk_count // (exp_local * groups))
    part_width = tokens.shape[1]
    both = jnp.concatenate([tokens, grad_output], axis=1)
    gathered = lax.all_to_all(
        jnp.broadcast_to(both[None], (groups,) + both.shape),
        "expert",
        split_axis=0,
        concat_axis=0,
        tiled=True,
    )
    gathered = gathered.reshape(groups, tok_local, 2, part_width)
    full_both = jnp.transpose(gathered, (1, 2, 0, 3)).reshape(tok_local, 2 * groups * part_width)
    feature_width = groups * part_width
    row_width = 2 * feature_width + PAD
    gate_piece = gate_weight[0]
    up_piece = up_weight[0]
    down_piece = down_weight[0]
    flat_ids = expert_ids.reshape(-1)
    row_count = flat_ids.shape[0]
    owned_rows = flat_ids // exp_local == group_index
    local_ids = flat_ids % exp_local
    chosen = (
        (local_ids[:, None] == jnp.arange(exp_local, dtype=jnp.int32)[None, :])
        & owned_rows[:, None]
    ).astype(jnp.int32)
    slot_ranks = jnp.sum(chosen * (jnp.cumsum(chosen, axis=0) - 1), axis=1)
    slot_count = exp_local * capacity
    slot_pos = jnp.where(owned_rows, local_ids * capacity + slot_ranks, slot_count)
    row_index = jnp.arange(row_count, dtype=jnp.int32)
    row_of = jnp.zeros((slot_count,), jnp.int32).at[slot_pos].set(row_index, mode="drop")
    slot_live = (
        jnp.zeros((slot_count,), jnp.int32).at[slot_pos].set(jnp.ones_like(row_index), mode="drop")
    )
    token_of = row_of // topk_count
    keep_mask = slot_live.astype(tokens.dtype)[:, None]
    slot_weight = route_weight.reshape(-1)[row_of] * slot_live.astype(route_weight.dtype)

    def spread(values):
        trailing = values.shape[1:]
        grouped = values.reshape((exp_local, 1, capacity) + trailing)
        return jnp.broadcast_to(grouped, (exp_local, chip_share, capacity) + trailing).reshape(
            (chips, capacity) + trailing
        )

    send_buf = jnp.concatenate(
        [full_both[token_of] * keep_mask, column_block(slot_weight, tokens.dtype)], axis=1
    )
    half_buf = lax.all_to_all(spread(send_buf), "dpc", split_axis=0, concat_axis=0, tiled=True)
    other_buf = lax.ppermute(half_buf, "core", [(k, (k + 1) % cores) for k in range(cores)])
    first = lax.axis_index("core") == 0
    recv_buf = jnp.where(
        first, jnp.stack([half_buf, other_buf]), jnp.stack([other_buf, half_buf])
    ).reshape(-1, row_width)
    slot_rows = recv_buf[:, :feature_width]
    slot_grads = recv_buf[:, feature_width : 2 * feature_width]
    slot_scale = recv_buf[:, 2 * feature_width]
    weight_wide = slot_scale.astype(jnp.float32)[:, None]

    gate_act = contract_last(slot_rows, gate_piece)
    up_act = contract_last(slot_rows, up_piece)
    active, silu_slope = silu_parts(gate_act)
    hidden = (active * up_act).astype(jnp.bfloat16)
    partial_out = jnp.dot(hidden, down_piece, preferred_element_type=jnp.float32)
    scaled = (weight_wide * partial_out).astype(jnp.bfloat16)

    into_hidden = contract_last(slot_grads, down_piece)
    route_terms = jnp.sum(into_hidden * hidden.astype(jnp.float32), axis=1).astype(jnp.bfloat16)
    hidden_grad = weight_wide * into_hidden
    gate_grad = (hidden_grad * up_act * silu_slope).astype(jnp.bfloat16)
    up_grad = (hidden_grad * active).astype(jnp.bfloat16)
    row_grad = (
        jnp.dot(gate_grad, gate_piece, preferred_element_type=jnp.float32)
        + jnp.dot(up_grad, up_piece, preferred_element_type=jnp.float32)
    ).astype(jnp.bfloat16)
    scaled_grad = (weight_wide * slot_grads.astype(jnp.float32)).astype(jnp.bfloat16)
    grad_gate = contract_first(gate_grad, slot_rows).astype(jnp.bfloat16)[None]
    grad_up = contract_first(up_grad, slot_rows).astype(jnp.bfloat16)[None]
    grad_down = contract_first(hidden, scaled_grad).astype(jnp.bfloat16)[None]

    core_index = lax.axis_index("core")
    piece_buf = jnp.concatenate([scaled, row_grad], axis=1).reshape(cores, -1, 2 * feature_width)
    pair = lax.all_to_all(piece_buf, "core", split_axis=0, concat_axis=0, tiled=True)
    pair_terms = lax.all_to_all(
        route_terms.reshape(cores, -1), "core", split_axis=0, concat_axis=0, tiled=True
    )
    pair_sum = jnp.sum(pair.astype(jnp.float32), axis=0).astype(jnp.bfloat16)
    lane = jnp.arange(PAD, dtype=jnp.int32)[None, :]
    term_block = jnp.zeros((pair_terms.shape[1], PAD), jnp.bfloat16)
    for k in range(cores):
        term_block = jnp.where(lane == k, pair_terms[k][:, None], term_block)
    back_buf = jnp.concatenate([pair_sum, term_block], axis=1)
    back = lax.all_to_all(
        back_buf.reshape(chips, capacity, row_width),
        "dpc",
        split_axis=0,
        concat_axis=0,
        tiled=True,
    ).reshape(-1, row_width)

    wide_token = spread(token_of).reshape(-1)
    wide_live = spread(slot_live).reshape(-1)
    wide_row = spread(row_of).reshape(-1)
    token_place = (
        (wide_token[None, :] == jnp.arange(tok_local, dtype=jnp.int32)[:, None])
        & (wide_live[None, :] > 0)
    ).astype(jnp.bfloat16)
    both_sum = jnp.dot(
        token_place, back[:, : 2 * feature_width], preferred_element_type=jnp.float32
    )
    row_place = (
        (wide_row[None, :] == jnp.arange(row_count, dtype=jnp.int32)[:, None])
        & (wide_live[None, :] > 0)
    ).astype(jnp.bfloat16)
    route_sum = jnp.dot(
        row_place,
        back[:, 2 * feature_width : 2 * feature_width + cores],
        preferred_element_type=jnp.float32,
    ).sum(axis=1)
    planes = jnp.transpose(
        both_sum.reshape(tok_local, 2, groups, part_width), (2, 0, 1, 3)
    ).reshape(groups, tok_local, 2 * part_width)
    route_row = jnp.pad(route_sum.reshape(groups, -1), ((0, 0), (0, 2 * part_width - row_count // groups)))
    packed = jnp.concatenate([planes, route_row[:, None]], axis=1).astype(jnp.bfloat16)
    received = lax.all_to_all(packed, "expert", split_axis=0, concat_axis=0, tiled=True)
    reduced = jnp.sum(received.astype(jnp.float32), axis=0)
    mixed_part = reduced[:tok_local, :part_width]
    token_part = reduced[:tok_local, part_width:]
    route_part = reduced[tok_local, : row_count // groups].reshape(-1, topk_count)
    return (
        mixed_part.astype(jnp.bfloat16),
        token_part.astype(jnp.bfloat16),
        route_part,
        grad_gate,
        grad_up,
        grad_down,
    )


def solution(mesh):
    devices = mesh.devices
    data_size, groups = devices.shape
    chip_mesh = Mesh(devices.reshape(data_size // 2, 2, groups), ("dpc", "core", "expert"))
    dp = ("dpc", "core")
    return jax.shard_map(
        on_device,
        mesh=chip_mesh,
        in_specs=(
            P(dp, "expert"),
            P(dp, None),
            P(dp, None),
            P("expert", dp, None),
            P("expert", dp, None),
            P("expert", dp, None),
            P(dp, "expert"),
        ),
        out_specs=(
            P(dp, "expert"),
            P(dp, "expert"),
            P(("dpc", "core", "expert"), None),
            P("expert", dp, None),
            P("expert", dp, None),
            P("expert", dp, None),
        ),
        check_vma=False,
    )
```

```python
import jax
import jax.numpy as jnp
from jax import lax
from jax.sharding import Mesh, PartitionSpec as P

PIECES = 4
PAD = 128


def contract_last(left_side, right_side):
    return lax.dot_general(
        left_side, right_side, (((1,), (1,)), ((), ())), preferred_element_type=jnp.float32
    )


def contract_first(left_side, right_side):
    return lax.dot_general(
        left_side, right_side, (((0,), (0,)), ((), ())), preferred_element_type=jnp.float32
    )


def silu_parts(gate_act):
    sigmoid_val = jax.nn.sigmoid(gate_act)
    return (gate_act * sigmoid_val, sigmoid_val * (1.0 + gate_act * (1.0 - sigmoid_val)))


def column_block(values, dtype):
    lane = jnp.arange(PAD, dtype=jnp.int32)[None, :] == 0
    return jnp.where(lane, values.astype(dtype)[:, None], jnp.zeros((), dtype))


def on_device(tokens, route_weight, expert_ids, gate_weight, up_weight, down_weight, grad_output):
    groups = lax.axis_size("expert")
    group_index = lax.axis_index("expert")
    chips = lax.axis_size("dpc")
    cores = lax.axis_size("core")
    data_size = chips * cores
    exp_local = data_size // PIECES
    chip_share = chips // exp_local
    tok_local, topk_count = expert_ids.shape
    capacity = min(tok_local, 2 * tok_local * topk_count // (exp_local * groups))
    part_width = tokens.shape[1]
    both = jnp.concatenate([tokens, grad_output], axis=1)
    gathered = lax.all_to_all(
        jnp.broadcast_to(both[None], (groups,) + both.shape),
        "expert",
        split_axis=0,
        concat_axis=0,
        tiled=True,
    )
    gathered = gathered.reshape(groups, tok_local, 2, part_width)
    full_both = jnp.transpose(gathered, (1, 2, 0, 3)).reshape(tok_local, 2 * groups * part_width)
    feature_width = groups * part_width
    row_width = 2 * feature_width + PAD
    gate_piece = gate_weight[0]
    up_piece = up_weight[0]
    down_piece = down_weight[0]
    flat_ids = expert_ids.reshape(-1)
    row_count = flat_ids.shape[0]
    owned_rows = flat_ids // exp_local == group_index
    local_ids = flat_ids % exp_local
    chosen = (
        (local_ids[:, None] == jnp.arange(exp_local, dtype=jnp.int32)[None, :])
        & owned_rows[:, None]
    ).astype(jnp.int32)
    slot_ranks = jnp.sum(chosen * (jnp.cumsum(chosen, axis=0) - 1), axis=1)
    slot_count = exp_local * capacity
    slot_pos = jnp.where(owned_rows, local_ids * capacity + slot_ranks, slot_count)
    row_index = jnp.arange(row_count, dtype=jnp.int32)
    row_of = jnp.zeros((slot_count,), jnp.int32).at[slot_pos].set(row_index, mode="drop")
    slot_live = (
        jnp.zeros((slot_count,), jnp.int32).at[slot_pos].set(jnp.ones_like(row_index), mode="drop")
    )
    token_of = row_of // topk_count
    keep_mask = slot_live.astype(tokens.dtype)[:, None]
    slot_weight = route_weight.reshape(-1)[row_of] * slot_live.astype(route_weight.dtype)

    def spread(values):
        trailing = values.shape[1:]
        grouped = values.reshape((exp_local, 1, capacity) + trailing)
        return jnp.broadcast_to(grouped, (exp_local, chip_share, capacity) + trailing).reshape(
            (chips, capacity) + trailing
        )

    send_buf = jnp.concatenate(
        [full_both[token_of] * keep_mask, column_block(slot_weight, tokens.dtype)], axis=1
    )
    half_buf = lax.all_to_all(spread(send_buf), "dpc", split_axis=0, concat_axis=0, tiled=True)
    other_buf = lax.ppermute(half_buf, "core", [(k, (k + 1) % cores) for k in range(cores)])
    first = lax.axis_index("core") == 0
    recv_buf = jnp.where(
        first, jnp.stack([half_buf, other_buf]), jnp.stack([other_buf, half_buf])
    ).reshape(-1, row_width)
    slot_rows = recv_buf[:, :feature_width]
    slot_grads = recv_buf[:, feature_width : 2 * feature_width]
    slot_scale = recv_buf[:, 2 * feature_width]
    weight_wide = slot_scale.astype(jnp.float32)[:, None]

    gate_act = contract_last(slot_rows, gate_piece)
    up_act = contract_last(slot_rows, up_piece)
    active, silu_slope = silu_parts(gate_act)
    hidden = (active * up_act).astype(jnp.bfloat16)
    partial_out = jnp.dot(hidden, down_piece, preferred_element_type=jnp.float32)
    scaled = (weight_wide * partial_out).astype(jnp.bfloat16)

    into_hidden = contract_last(slot_grads, down_piece)
    route_terms = jnp.sum(into_hidden * hidden.astype(jnp.float32), axis=1).astype(jnp.bfloat16)
    hidden_grad = weight_wide * into_hidden
    gate_grad = (hidden_grad * up_act * silu_slope).astype(jnp.bfloat16)
    up_grad = (hidden_grad * active).astype(jnp.bfloat16)
    row_grad = (
        jnp.dot(gate_grad, gate_piece, preferred_element_type=jnp.float32)
        + jnp.dot(up_grad, up_piece, preferred_element_type=jnp.float32)
    ).astype(jnp.bfloat16)
    scaled_grad = (weight_wide * slot_grads.astype(jnp.float32)).astype(jnp.bfloat16)
    grad_gate = contract_first(gate_grad, slot_rows).astype(jnp.bfloat16)[None]
    grad_up = contract_first(up_grad, slot_rows).astype(jnp.bfloat16)[None]
    grad_down = contract_first(hidden, scaled_grad).astype(jnp.bfloat16)[None]

    piece_buf = jnp.concatenate(
        [scaled, row_grad, column_block(route_terms, jnp.bfloat16)], axis=1
    ).reshape(cores, -1, row_width)
    mine = jnp.where(first, piece_buf[0], piece_buf[1])
    got = lax.ppermute(
        jnp.where(first, piece_buf[1], piece_buf[0]),
        "core",
        [(k, (k + 1) % cores) for k in range(cores)],
    )
    pair_sum = (
        mine[:, : 2 * feature_width].astype(jnp.float32) + got[:, : 2 * feature_width].astype(jnp.float32)
    ).astype(jnp.bfloat16)
    lane = jnp.arange(PAD, dtype=jnp.int32)[None, :]
    term_col = 2 * feature_width
    term_block = jnp.where(
        lane == 0,
        mine[:, term_col : term_col + 1],
        jnp.where(lane == 1, got[:, term_col : term_col + 1], jnp.zeros((), jnp.bfloat16)),
    )
    back_buf = jnp.concatenate([pair_sum, term_block], axis=1)
    back = lax.all_to_all(
        back_buf.reshape(chips, capacity, row_width),
        "dpc",
        split_axis=0,
        concat_axis=0,
        tiled=True,
    ).reshape(-1, row_width)

    wide_token = spread(token_of).reshape(-1)
    wide_live = spread(slot_live).reshape(-1)
    wide_row = spread(row_of).reshape(-1)
    token_place = (
        (wide_token[None, :] == jnp.arange(tok_local, dtype=jnp.int32)[:, None])
        & (wide_live[None, :] > 0)
    ).astype(jnp.bfloat16)
    both_sum = jnp.dot(
        token_place, back[:, : 2 * feature_width], preferred_element_type=jnp.float32
    )
    row_place = (
        (wide_row[None, :] == jnp.arange(row_count, dtype=jnp.int32)[:, None])
        & (wide_live[None, :] > 0)
    ).astype(jnp.bfloat16)
    route_sum = jnp.dot(
        row_place,
        back[:, 2 * feature_width : 2 * feature_width + cores],
        preferred_element_type=jnp.float32,
    ).sum(axis=1)
    planes = jnp.transpose(
        both_sum.reshape(tok_local, 2, groups, part_width), (2, 0, 1, 3)
    ).reshape(groups, tok_local, 2 * part_width)
    route_row = jnp.pad(route_sum.reshape(groups, -1), ((0, 0), (0, 2 * part_width - row_count // groups)))
    packed = jnp.concatenate([planes, route_row[:, None]], axis=1).astype(jnp.bfloat16)
    received = lax.all_to_all(packed, "expert", split_axis=0, concat_axis=0, tiled=True)
    reduced = jnp.sum(received.astype(jnp.float32), axis=0)
    mixed_part = reduced[:tok_local, :part_width]
    token_part = reduced[:tok_local, part_width:]
    route_part = reduced[tok_local, : row_count // groups].reshape(-1, topk_count)
    return (
        mixed_part.astype(jnp.bfloat16),
        token_part.astype(jnp.bfloat16),
        route_part,
        grad_gate,
        grad_up,
        grad_down,
    )


def solution(mesh):
    devices = mesh.devices
    data_size, groups = devices.shape
    chip_mesh = Mesh(devices.reshape(data_size // 2, 2, groups), ("dpc", "core", "expert"))
    dp = ("dpc", "core")
    return jax.shard_map(
        on_device,
        mesh=chip_mesh,
        in_specs=(
            P(dp, "expert"),
            P(dp, None),
            P(dp, None),
            P("expert", dp, None),
            P("expert", dp, None),
            P("expert", dp, None),
            P(dp, "expert"),
        ),
        out_specs=(
            P(dp, "expert"),
            P(dp, "expert"),
            P(("dpc", "core", "expert"), None),
            P("expert", dp, None),
            P("expert", dp, None),
            P("expert", dp, None),
        ),
        check_vma=False,
    )
```

```python
import jax
import jax.numpy as jnp
from jax import lax
from jax.sharding import Mesh, PartitionSpec as P

PIECES = 4
PAD = 128


def contract_last(left_side, right_side):
    return lax.dot_general(
        left_side, right_side, (((1,), (1,)), ((), ())), preferred_element_type=jnp.float32
    )


def contract_first(left_side, right_side):
    return lax.dot_general(
        left_side, right_side, (((0,), (0,)), ((), ())), preferred_element_type=jnp.float32
    )


def silu_parts(gate_act):
    sigmoid_val = jax.nn.sigmoid(gate_act)
    return (gate_act * sigmoid_val, sigmoid_val * (1.0 + gate_act * (1.0 - sigmoid_val)))


def column_block(values, dtype):
    lane = jnp.arange(PAD, dtype=jnp.int32)[None, :] == 0
    return jnp.where(lane, values.astype(dtype)[:, None], jnp.zeros((), dtype))


def on_device(tokens, route_weight, expert_ids, gate_weight, up_weight, down_weight, grad_output):
    groups = lax.axis_size("expert")
    group_index = lax.axis_index("expert")
    chips = lax.axis_size("dpc")
    cores = lax.axis_size("core")
    data_size = chips * cores
    exp_local = data_size // PIECES
    chip_share = chips // exp_local
    tok_local, topk_count = expert_ids.shape
    capacity = min(tok_local, 2 * tok_local * topk_count // (exp_local * groups))
    part_width = tokens.shape[1]
    both = jnp.concatenate([tokens, grad_output], axis=1)
    gathered = lax.all_to_all(
        jnp.broadcast_to(both[None], (groups,) + both.shape),
        "expert",
        split_axis=0,
        concat_axis=0,
        tiled=True,
    )
    gathered = gathered.reshape(groups, tok_local, 2, part_width)
    full_both = jnp.transpose(gathered, (1, 2, 0, 3)).reshape(tok_local, 2 * groups * part_width)
    feature_width = groups * part_width
    row_width = 2 * feature_width + PAD
    gate_piece = gate_weight[0]
    up_piece = up_weight[0]
    down_piece = down_weight[0]
    flat_ids = expert_ids.reshape(-1)
    row_count = flat_ids.shape[0]
    owned_rows = flat_ids // exp_local == group_index
    local_ids = flat_ids % exp_local
    chosen = (
        (local_ids[:, None] == jnp.arange(exp_local, dtype=jnp.int32)[None, :])
        & owned_rows[:, None]
    ).astype(jnp.int32)
    slot_ranks = jnp.sum(chosen * (jnp.cumsum(chosen, axis=0) - 1), axis=1)
    slot_count = exp_local * capacity
    slot_pos = jnp.where(owned_rows, local_ids * capacity + slot_ranks, slot_count)
    row_index = jnp.arange(row_count, dtype=jnp.int32)
    row_of = jnp.zeros((slot_count,), jnp.int32).at[slot_pos].set(row_index, mode="drop")
    slot_live = (
        jnp.zeros((slot_count,), jnp.int32).at[slot_pos].set(jnp.ones_like(row_index), mode="drop")
    )
    token_of = row_of // topk_count
    keep_mask = slot_live.astype(tokens.dtype)[:, None]
    slot_weight = route_weight.reshape(-1)[row_of] * slot_live.astype(route_weight.dtype)

    def spread(values):
        trailing = values.shape[1:]
        grouped = values.reshape((exp_local, 1, capacity) + trailing)
        return jnp.broadcast_to(grouped, (exp_local, chip_share, capacity) + trailing).reshape(
            (chips, capacity) + trailing
        )

    send_buf = jnp.concatenate(
        [full_both[token_of] * keep_mask, column_block(slot_weight, tokens.dtype)], axis=1
    )
    half_buf = lax.all_to_all(spread(send_buf), "dpc", split_axis=0, concat_axis=0, tiled=True)
    other_buf = lax.ppermute(half_buf, "core", [(k, (k + 1) % cores) for k in range(cores)])
    recv_buf = jnp.stack([half_buf, other_buf]).reshape(-1, row_width)
    slot_rows = recv_buf[:, :feature_width]
    slot_grads = recv_buf[:, feature_width : 2 * feature_width]
    slot_scale = recv_buf[:, 2 * feature_width]
    weight_wide = slot_scale.astype(jnp.float32)[:, None]

    gate_act = contract_last(slot_rows, gate_piece)
    up_act = contract_last(slot_rows, up_piece)
    active, silu_slope = silu_parts(gate_act)
    hidden = (active * up_act).astype(jnp.bfloat16)
    partial_out = jnp.dot(hidden, down_piece, preferred_element_type=jnp.float32)
    scaled = (weight_wide * partial_out).astype(jnp.bfloat16)

    into_hidden = contract_last(slot_grads, down_piece)
    route_terms = jnp.sum(into_hidden * hidden.astype(jnp.float32), axis=1).astype(jnp.bfloat16)
    hidden_grad = weight_wide * into_hidden
    gate_grad = (hidden_grad * up_act * silu_slope).astype(jnp.bfloat16)
    up_grad = (hidden_grad * active).astype(jnp.bfloat16)
    row_grad = (
        jnp.dot(gate_grad, gate_piece, preferred_element_type=jnp.float32)
        + jnp.dot(up_grad, up_piece, preferred_element_type=jnp.float32)
    ).astype(jnp.bfloat16)
    scaled_grad = (weight_wide * slot_grads.astype(jnp.float32)).astype(jnp.bfloat16)
    grad_gate = contract_first(gate_grad, slot_rows).astype(jnp.bfloat16)[None]
    grad_up = contract_first(up_grad, slot_rows).astype(jnp.bfloat16)[None]
    grad_down = contract_first(hidden, scaled_grad).astype(jnp.bfloat16)[None]

    piece_buf = jnp.concatenate(
        [scaled, row_grad, column_block(route_terms, jnp.bfloat16)], axis=1
    ).reshape(cores, -1, row_width)
    mine = piece_buf[0]
    got = lax.ppermute(
        piece_buf[1],
        "core",
        [(k, (k + 1) % cores) for k in range(cores)],
    )
    pair_sum = (
        mine[:, : 2 * feature_width].astype(jnp.float32) + got[:, : 2 * feature_width].astype(jnp.float32)
    ).astype(jnp.bfloat16)
    lane = jnp.arange(PAD, dtype=jnp.int32)[None, :]
    term_col = 2 * feature_width
    term_block = jnp.where(
        lane == 0,
        mine[:, term_col : term_col + 1],
        jnp.where(lane == 1, got[:, term_col : term_col + 1], jnp.zeros((), jnp.bfloat16)),
    )
    back_buf = jnp.concatenate([pair_sum, term_block], axis=1)
    back = lax.all_to_all(
        back_buf.reshape(chips, capacity, row_width),
        "dpc",
        split_axis=0,
        concat_axis=0,
        tiled=True,
    ).reshape(-1, row_width)

    wide_token = spread(token_of).reshape(-1)
    wide_live = spread(slot_live).reshape(-1)
    wide_row = spread(row_of).reshape(-1)
    token_place = (
        (wide_token[None, :] == jnp.arange(tok_local, dtype=jnp.int32)[:, None])
        & (wide_live[None, :] > 0)
    ).astype(jnp.bfloat16)
    both_sum = jnp.dot(
        token_place, back[:, : 2 * feature_width], preferred_element_type=jnp.float32
    )
    row_place = (
        (wide_row[None, :] == jnp.arange(row_count, dtype=jnp.int32)[:, None])
        & (wide_live[None, :] > 0)
    ).astype(jnp.bfloat16)
    route_sum = jnp.dot(
        row_place,
        back[:, 2 * feature_width : 2 * feature_width + cores],
        preferred_element_type=jnp.float32,
    ).sum(axis=1)
    planes = jnp.transpose(
        both_sum.reshape(tok_local, 2, groups, part_width), (2, 0, 1, 3)
    ).reshape(groups, tok_local, 2 * part_width)
    route_row = jnp.pad(route_sum.reshape(groups, -1), ((0, 0), (0, 2 * part_width - row_count // groups)))
    packed = jnp.concatenate([planes, route_row[:, None]], axis=1).astype(jnp.bfloat16)
    received = lax.all_to_all(packed, "expert", split_axis=0, concat_axis=0, tiled=True)
    reduced = jnp.sum(received.astype(jnp.float32), axis=0)
    mixed_part = reduced[:tok_local, :part_width]
    token_part = reduced[:tok_local, part_width:]
    route_part = reduced[tok_local, : row_count // groups].reshape(-1, topk_count)
    return (
        mixed_part.astype(jnp.bfloat16),
        token_part.astype(jnp.bfloat16),
        route_part,
        grad_gate,
        grad_up,
        grad_down,
    )


def solution(mesh):
    devices = mesh.devices
    data_size, groups = devices.shape
    chip_mesh = Mesh(devices.reshape(data_size // 2, 2, groups), ("dpc", "core", "expert"))
    dp = ("dpc", "core")
    return jax.shard_map(
        on_device,
        mesh=chip_mesh,
        in_specs=(
            P(dp, "expert"),
            P(dp, None),
            P(dp, None),
            P("expert", dp, None),
            P("expert", dp, None),
            P("expert", dp, None),
            P(dp, "expert"),
        ),
        out_specs=(
            P(dp, "expert"),
            P(dp, "expert"),
            P(("dpc", "core", "expert"), None),
            P("expert", dp, None),
            P("expert", dp, None),
            P("expert", dp, None),
        ),
        check_vma=False,
    )
```
